256 devices in a mesh: pos: 16 (over x_hi, z), exp: 16 (over y, x_lo, core).
Axes of the slice: x: 4 (x_hi: 2, x_lo: 2; x = x_hi * 2 + x_lo), y: 4, z: 8, core: 2. Of those that a mesh axis runs over, the one named last changes fastest.
Arguments:
- patches: bfloat16 [65536, 4, 256], P(('pos', 'exp')), may hold values from -6 to 6
- conv_weight: bfloat16 [3, 256, 2048], replicated, may hold values from -0.21875 to 0.21875
- phi: bfloat16 [2048, 128], replicated, may hold values from -40 to 40, as said below
- w_in: bfloat16 [16, 2048, 8192], P('exp', None, 'pos'), may hold values from -0.125 to 0.125
- w_out: bfloat16 [16, 8192, 2048], P('exp', 'pos'), may hold values from -0.0625 to 0.0625
Outputs:
- mixed: bfloat16 [65536, 4, 2048], P(('pos', 'exp'))
The draws below stay inside these ranges and needn't reach their ends.
Inputs may be any that keep to these rules, and one draw needn't show every extreme that they name: phi is real-valued.
All inputs are finite; a program needn't handle non-finite values.
Results may differ from the reference program's by a relative error of at most 0.019.
The reference program's roundings to bfloat16 on the way (of `tokens`, `dispatch`, `slot_in`, `hidden`, `slot_out` and `combine`) count: a program that leaves them out, or rounds other values in their place, can miss the bound.
Values may be sent and summed in bfloat16 or wider, within the bound.
No kernel may reach another device: no remote copies, remote signals or barrier semaphores. Data moves between devices by JAX's collectives and lax.ppermute only.
A program may use at most 128 MiB of HBM per device.

```python
import math
import jax
import jax.numpy as jnp
from jax import lax

D = 2048
FF = 8192
PATCH = 256
SLOTS_PER = 8
TP = 4
CH = 65536
EXPERTS = 16
SLOTS = 128


def draw_phi(key, part):
    first_key, second_key = jax.random.split(key, 2)
    base = jnp.clip(jax.random.normal(first_key, (D, SLOTS), jnp.float32), -5.0, 5.0)
    scale = jnp.exp(jax.random.uniform(second_key, (1, SLOTS), jnp.float32, math.log(3.0), math.log(4.5)))
    return jnp.clip(base * scale * (2.0 / math.sqrt(D)), -40.0, 40.0).astype(jnp.bfloat16)


def level_of(own_key, extent, cuts, least, largest):
    loudness = 1.0
    for dim, parts in cuts:
        draws = jax.random.uniform(jax.random.fold_in(jax.random.fold_in(own_key, 6), dim), (parts,), jnp.float32, least / len(cuts), largest / len(cuts))
        loudness = loudness * jnp.repeat(jnp.exp(draws), extent[dim] // parts).reshape((-1,) + (1,) * (len(extent) - 1 - dim))
    return loudness


def normal_values(own_key, dims, scale, limit, shards=(), kind=jnp.bfloat16):
    drawn = jax.random.normal(own_key, dims, jnp.float32) * scale
    if len(shards) > 0:
        drawn = level_of(own_key, dims, shards, -0.22, 0.18) * drawn
    return jnp.clip(drawn, min=-limit, max=limit).astype(kind)


def setup_inputs(seed: int = 0) -> dict:
    key_of = jax.random.split(jax.random.key(seed), 6)
    patches = normal_values(key_of[0], (CH, TP, PATCH), 1.0, 6.0, ((0, 256),))
    conv_weight = normal_values(key_of[1], (3, PATCH, D), (3 * PATCH) ** -0.5, 0.21875)
    phi = draw_phi(jax.random.fold_in(key_of[5], 71), 0)
    w_in = normal_values(key_of[3], (EXPERTS, D, FF), D ** -0.5, 0.125, ((0, 16), (2, 16)))
    w_out = normal_values(key_of[4], (EXPERTS, FF, D), FF ** -0.5, 0.0625, ((0, 16), (1, 16)))
    return dict(patches=patches, conv_weight=conv_weight, phi=phi, w_in=w_in, w_out=w_out)


def reference(patches, conv_weight, phi, w_in, w_out):
    padded = jnp.pad(patches, ((1, 1), (0, 0), (0, 0)))

    def encode(channel):
        rows = lax.dynamic_slice_in_dim(padded, channel, 3, 0)
        running = jnp.zeros((TP, D), jnp.float32)
        for offset in range(3):
            running = running + jnp.dot(rows[offset], conv_weight[offset], preferred_element_type=jnp.float32)
        return running.astype(jnp.bfloat16)

    tokens = lax.map(encode, jnp.arange(CH, dtype=jnp.int32))
    flat = tokens.reshape(CH * TP, D)
    logits = jnp.dot(flat, phi, preferred_element_type=jnp.float32)
    column_peak = jnp.max(logits, axis=0)
    raw_weights = jnp.exp(logits - column_peak)
    column_total = jnp.sum(raw_weights, axis=0)
    dispatch = (raw_weights / column_total).astype(jnp.bfloat16)
    slot_in = lax.dot_general(dispatch, flat, (((0,), (0,)), ((), ())), preferred_element_type=jnp.float32).astype(jnp.bfloat16)

    def expert(inputs):
        rows, first, second = inputs
        hidden = jax.nn.gelu(jnp.dot(rows, first, preferred_element_type=jnp.float32), approximate=True).astype(jnp.bfloat16)
        return jnp.dot(hidden, second, preferred_element_type=jnp.float32).astype(jnp.bfloat16)

    slot_out = lax.map(expert, (slot_in.reshape(EXPERTS, SLOTS_PER, D), w_in, w_out)).reshape(SLOTS, D)
    row_peak = jnp.max(logits, axis=1, keepdims=True)
    row_weights = jnp.exp(logits - row_peak)
    combine = (row_weights / jnp.sum(row_weights, axis=1, keepdims=True)).astype(jnp.bfloat16)
    mixed = jnp.dot(combine, slot_out, preferred_element_type=jnp.float32).astype(jnp.bfloat16)
    return mixed.reshape(CH, TP, D)
```

```python
import jax
import jax.numpy as jnp
from jax import lax
from jax.sharding import PartitionSpec as P

D = 2048
SLOTS_PER = 8


def with_halo(array, sides, width):
    for axis, dim in sides:
        count, length = (lax.axis_size(axis), array.shape[dim])
        up = [(i, (i + 1) % count) for i in range(count - 1)]
        down = [(j, i) for i, j in up]
        last = lax.slice_in_dim(array, length - width, length, axis=dim)
        initial = lax.slice_in_dim(array, 0, width, axis=dim)
        before = lax.ppermute(last, axis, up)
        after = lax.ppermute(initial, axis, down)
        array = jnp.concatenate([before, array, after], axis=dim)
    return array


def butterfly_sum(value, axis):
    count = lax.axis_size(axis)
    step = 1
    while step < count:
        pairs = [(i, i ^ step) for i in range(count)]
        value = value + lax.ppermute(value, axis, pairs)
        step *= 2
    return value


def gather_rows(row, axes):
    count = lax.axis_size(axes)
    tiled = jnp.broadcast_to(row[None, :], (count, row.shape[0]))
    return lax.all_to_all(tiled, axes, 0, 0, tiled=True)


def per_device(patches, conv_weight, phi, w_in, w_out):
    channels, periods, samples = patches.shape
    every = ("pos", "exp")
    padded = with_halo(patches, ((every, 0),), 1)
    running = jnp.zeros((channels * periods, D), jnp.float32)
    for offset in range(3):
        window = padded[offset : offset + channels].reshape(channels * periods, samples)
        running = running + jnp.dot(window, conv_weight[offset], preferred_element_type=jnp.float32)
    flat = running.astype(jnp.bfloat16)
    logits = jnp.dot(flat, phi, preferred_element_type=jnp.float32)
    slots = logits.shape[1]

    local_peak = jnp.max(logits, axis=0)
    local_total = jnp.sum(jnp.exp(logits - local_peak), axis=0)
    stats = gather_rows(jnp.concatenate([local_peak, local_total]), every)
    peaks, totals = stats[:, :slots], stats[:, slots:]
    column_peak = jnp.max(peaks, axis=0)
    column_total = jnp.sum(totals * jnp.exp(peaks - column_peak), axis=0)

    raw_weights = jnp.exp(logits - column_peak)
    dispatch = (raw_weights / column_total).astype(jnp.bfloat16)
    every_slot = lax.dot_general(
        dispatch, flat, (((0,), (0,)), ((), ())), preferred_element_type=jnp.float32
    )
    groups = lax.axis_size("exp")
    mine = lax.all_to_all(every_slot, "exp", 0, 0, tiled=True)
    owned = jnp.sum(mine.reshape(groups, SLOTS_PER, D), axis=0)
    slot_in = butterfly_sum(owned, "pos").astype(jnp.bfloat16)
    hidden = jax.nn.gelu(
        jnp.dot(slot_in, w_in[0], preferred_element_type=jnp.float32), approximate=True
    ).astype(jnp.bfloat16)
    expert_term = jnp.dot(hidden, w_out[0], preferred_element_type=jnp.float32)
    slot_out = butterfly_sum(expert_term, "pos").astype(jnp.bfloat16)
    row_peak = jnp.max(logits, axis=1, keepdims=True)
    row_weights = jnp.exp(logits - row_peak)
    combine = (row_weights / jnp.sum(row_weights, axis=1, keepdims=True)).astype(jnp.bfloat16)
    mixed = jnp.dot(
        combine,
        lax.all_gather(slot_out, "exp", axis=0, tiled=True),
        preferred_element_type=jnp.float32,
    )
    return mixed.astype(jnp.bfloat16).reshape(channels, periods, D)


def solution(mesh):
    in_specs = (
        P(("pos", "exp"), None, None),
        P(),
        P(),
        P("exp", None, "pos"),
        P("exp", "pos", None),
    )
    out_specs = P(("pos", "exp"), None, None)
    return jax.shard_map(
        per_device, mesh=mesh, in_specs=in_specs, out_specs=out_specs, check_vma=False
    )
```

```python
import jax
import jax.numpy as jnp
from jax import lax
from jax.sharding import PartitionSpec as P

D = 2048
SLOTS_PER = 8


def with_halo(array, sides, width):
    for axis, dim in sides:
        count, length = (lax.axis_size(axis), array.shape[dim])
        up = [(i, (i + 1) % count) for i in range(count - 1)]
        down = [(j, i) for i, j in up]
        last = lax.slice_in_dim(array, length - width, length, axis=dim)
        initial = lax.slice_in_dim(array, 0, width, axis=dim)
        before = lax.ppermute(last, axis, up)
        after = lax.ppermute(initial, axis, down)
        array = jnp.concatenate([before, array, after], axis=dim)
    return array


def butterfly_sum(value, axis):
    count = lax.axis_size(axis)
    step = 1
    while step < count:
        pairs = [(i, i ^ step) for i in range(count)]
        value = value + lax.ppermute(value, axis, pairs)
        step *= 2
    return value


def merge(mine, theirs):
    peak = jnp.maximum(mine[:, D], theirs[:, D])
    a = jnp.exp(mine[:, D] - peak)[:, None]
    b = jnp.exp(theirs[:, D] - peak)[:, None]
    merged = mine * a + theirs * b
    return merged.at[:, D].set(peak)


def butterfly_softmax_sum(value, axis):
    count = lax.axis_size(axis)
    step = 1
    while step < count:
        pairs = [(i, i ^ step) for i in range(count)]
        value = merge(value, lax.ppermute(value, axis, pairs))
        step *= 2
    return value


def per_device(patches, conv_weight, phi, w_in, w_out):
    channels, periods, samples = patches.shape
    every = ("pos", "exp")
    padded = with_halo(patches, ((every, 0),), 1)
    running = jnp.zeros((channels * periods, D), jnp.float32)
    for offset in range(3):
        window = padded[offset : offset + channels].reshape(channels * periods, samples)
        running = running + jnp.dot(window, conv_weight[offset], preferred_element_type=jnp.float32)
    flat = running.astype(jnp.bfloat16)
    logits = jnp.dot(flat, phi, preferred_element_type=jnp.float32)
    slots = logits.shape[1]

    local_peak = jnp.max(logits, axis=0)
    raw_weights = jnp.exp(logits - local_peak)
    local_total = jnp.sum(raw_weights, axis=0)
    every_slot = lax.dot_general(
        raw_weights.astype(jnp.bfloat16), flat, (((0,), (0,)), ((), ())),
        preferred_element_type=jnp.float32,
    )
    extra = jnp.zeros((slots, 128), jnp.float32)
    extra = extra.at[:, 0].set(local_peak).at[:, 1].set(local_total)
    packed = jnp.concatenate([every_slot, extra], axis=1)
    groups = lax.axis_size("exp")
    mine = lax.all_to_all(packed, "exp", 0, 0, tiled=True).reshape(groups, SLOTS_PER, -1)
    peaks = mine[:, :, D]
    peak = jnp.max(peaks, axis=0)
    scale = jnp.exp(peaks - peak)
    sums = jnp.sum(mine[:, :, :D] * scale[:, :, None], axis=0)
    total = jnp.sum(mine[:, :, D + 1] * scale, axis=0)
    owned = jnp.concatenate(
        [sums, jnp.zeros((SLOTS_PER, 128), jnp.float32).at[:, 0].set(peak).at[:, 1].set(total)], axis=1
    )
    owned = butterfly_softmax_sum(owned, "pos")
    slot_in = (owned[:, :D] / owned[:, D + 1 : D + 2]).astype(jnp.bfloat16)
    hidden = jax.nn.gelu(
        jnp.dot(slot_in, w_in[0], preferred_element_type=jnp.float32), approximate=True
    ).astype(jnp.bfloat16)
    expert_term = jnp.dot(hidden, w_out[0], preferred_element_type=jnp.float32)
    slot_out = butterfly_sum(expert_term, "pos").astype(jnp.bfloat16)
    row_peak = jnp.max(logits, axis=1, keepdims=True)
    row_weights = jnp.exp(logits - row_peak)
    combine = (row_weights / jnp.sum(row_weights, axis=1, keepdims=True)).astype(jnp.bfloat16)
    mixed = jnp.dot(
        combine,
        lax.all_gather(slot_out, "exp", axis=0, tiled=True),
        preferred_element_type=jnp.float32,
    )
    return mixed.astype(jnp.bfloat16).reshape(channels, periods, D)


def solution(mesh):
    in_specs = (
        P(("pos", "exp"), None, None),
        P(),
        P(),
        P("exp", None, "pos"),
        P("exp", "pos", None),
    )
    out_specs = P(("pos", "exp"), None, None)
    return jax.shard_map(
        per_device, mesh=mesh, in_specs=in_specs, out_specs=out_specs, check_vma=False
    )
```

```python
import jax
import jax.numpy as jnp
from jax import lax
from jax.sharding import PartitionSpec as P

D = 2048
SLOTS_PER = 8


def with_halo(array, sides, width):
    for axis, dim in sides:
        count, length = (lax.axis_size(axis), array.shape[dim])
        up = [(i, (i + 1) % count) for i in range(count - 1)]
        down = [(j, i) for i, j in up]
        last = lax.slice_in_dim(array, length - width, length, axis=dim)
        initial = lax.slice_in_dim(array, 0, width, axis=dim)
        before = lax.ppermute(last, axis, up)
        after = lax.ppermute(initial, axis, down)
        array = jnp.concatenate([before, array, after], axis=dim)
    return array


def butterfly_sum(value, axis):
    count = lax.axis_size(axis)
    step = 1
    while step < count:
        pairs = [(i, i ^ step) for i in range(count)]
        value = value + lax.ppermute(value, axis, pairs)
        step *= 2
    return value


def merge(mine, theirs):
    peak = jnp.maximum(mine[:, D], theirs[:, D])
    a = jnp.exp(mine[:, D] - peak)[:, None]
    b = jnp.exp(theirs[:, D] - peak)[:, None]
    merged = mine * a + theirs * b
    return merged.at[:, D].set(peak)


def butterfly_softmax_sum(value, axis):
    count = lax.axis_size(axis)
    step = 1
    while step < count:
        pairs = [(i, i ^ step) for i in range(count)]
        value = merge(value, lax.ppermute(value, axis, pairs))
        step *= 2
    return value


def per_device(patches, conv_weight, phi, w_in, w_out):
    channels, periods, samples = patches.shape
    every = ("pos", "exp")
    padded = with_halo(patches, ((every, 0),), 1)
    window = jnp.concatenate([padded[offset : offset + channels] for offset in range(3)], axis=2)
    taps = conv_weight.reshape(3 * samples, D)
    window = window.reshape(channels * periods, 3 * samples)
    flat = jnp.dot(window, taps, preferred_element_type=jnp.float32).astype(jnp.bfloat16)
    logits = jnp.dot(flat, phi, preferred_element_type=jnp.float32)
    slots = logits.shape[1]

    local_peak = jnp.max(logits, axis=0)
    raw_weights = jnp.exp(logits - local_peak)
    local_total = jnp.sum(raw_weights, axis=0)
    every_slot = lax.dot_general(
        raw_weights.astype(jnp.bfloat16), flat, (((0,), (0,)), ((), ())),
        preferred_element_type=jnp.float32,
    )
    extra = jnp.zeros((slots, 128), jnp.float32)
    extra = extra.at[:, 0].set(local_peak).at[:, 1].set(local_total)
    packed = jnp.concatenate([every_slot, extra], axis=1)
    groups = lax.axis_size("exp")
    mine = lax.all_to_all(packed, "exp", 0, 0, tiled=True).reshape(groups, SLOTS_PER, -1)
    peaks = mine[:, :, D]
    peak = jnp.max(peaks, axis=0)
    scale = jnp.exp(peaks - peak)
    sums = jnp.sum(mine[:, :, :D] * scale[:, :, None], axis=0)
    total = jnp.sum(mine[:, :, D + 1] * scale, axis=0)
    owned = jnp.concatenate(
        [sums, jnp.zeros((SLOTS_PER, 128), jnp.float32).at[:, 0].set(peak).at[:, 1].set(total)], axis=1
    )
    owned = butterfly_softmax_sum(owned, "pos")
    slot_in = (owned[:, :D] / owned[:, D + 1 : D + 2]).astype(jnp.bfloat16)
    hidden = jax.nn.gelu(
        jnp.dot(slot_in, w_in[0], preferred_element_type=jnp.float32), approximate=True
    ).astype(jnp.bfloat16)
    expert_term = jnp.dot(hidden, w_out[0], preferred_element_type=jnp.float32)
    slot_out = butterfly_sum(expert_term, "pos").astype(jnp.bfloat16)
    row_peak = jnp.max(logits, axis=1, keepdims=True)
    row_weights = jnp.exp(logits - row_peak)
    combine = (row_weights / jnp.sum(row_weights, axis=1, keepdims=True)).astype(jnp.bfloat16)
    mixed = jnp.dot(
        combine,
        lax.all_gather(slot_out, "exp", axis=0, tiled=True),
        preferred_element_type=jnp.float32,
    )
    return mixed.astype(jnp.bfloat16).reshape(channels, periods, D)


def solution(mesh):
    in_specs = (
        P(("pos", "exp"), None, None),
        P(),
        P(),
        P("exp", None, "pos"),
        P("exp", "pos", None),
    )
    out_specs = P(("pos", "exp"), None, None)
    return jax.shard_map(
        per_device, mesh=mesh, in_specs=in_specs, out_specs=out_specs, check_vma=False
    )
```

```python
import jax
import jax.numpy as jnp
from jax import lax
from jax.sharding import PartitionSpec as P

D = 2048
SLOTS_PER = 8


def with_halo(array, sides, width):
    for axis, dim in sides:
        count, length = (lax.axis_size(axis), array.shape[dim])
        up = [(i, (i + 1) % count) for i in range(count - 1)]
        down = [(j, i) for i, j in up]
        last = lax.slice_in_dim(array, length - width, length, axis=dim)
        initial = lax.slice_in_dim(array, 0, width, axis=dim)
        before = lax.ppermute(last, axis, up)
        after = lax.ppermute(initial, axis, down)
        array = jnp.concatenate([before, array, after], axis=dim)
    return array


def butterfly_sum(value, axis):
    count = lax.axis_size(axis)
    step = 1
    while step < count:
        pairs = [(i, i ^ step) for i in range(count)]
        value = value + lax.ppermute(value, axis, pairs)
        step *= 2
    return value


def merge(mine, theirs):
    peak = jnp.maximum(mine[:, D], theirs[:, D])
    a = jnp.exp(mine[:, D] - peak)[:, None]
    b = jnp.exp(theirs[:, D] - peak)[:, None]
    merged = mine * a + theirs * b
    return merged.at[:, D].set(peak)


def butterfly_softmax_sum(value, axis):
    count = lax.axis_size(axis)
    step = 1
    while step < count:
        pairs = [(i, i ^ step) for i in range(count)]
        value = merge(value, lax.ppermute(value, axis, pairs))
        step *= 2
    return value


def per_device(patches, conv_weight, phi, w_in, w_out):
    channels, periods, samples = patches.shape
    every = ("pos", "exp")
    padded = with_halo(jnp.swapaxes(patches, 0, 1), ((every, 1),), 1)
    window = jnp.concatenate([padded[:, offset : offset + channels] for offset in range(3)], axis=2)
    window = window.reshape(periods * channels, 3 * samples)
    taps = conv_weight.reshape(3 * samples, D)
    flat = jnp.dot(window, taps, preferred_element_type=jnp.float32).astype(jnp.bfloat16)
    logits = jnp.dot(flat, phi, preferred_element_type=jnp.float32)
    slots = logits.shape[1]

    local_peak = jnp.max(logits, axis=0)
    raw_weights = jnp.exp(logits - local_peak)
    local_total = jnp.sum(raw_weights, axis=0)
    every_slot = lax.dot_general(
        raw_weights.astype(jnp.bfloat16), flat, (((0,), (0,)), ((), ())),
        preferred_element_type=jnp.float32,
    )
    extra = jnp.zeros((slots, 128), jnp.float32)
    extra = extra.at[:, 0].set(local_peak).at[:, 1].set(local_total)
    packed = jnp.concatenate([every_slot, extra], axis=1)
    groups = lax.axis_size("exp")
    mine = lax.all_to_all(packed, "exp", 0, 0, tiled=True).reshape(groups, SLOTS_PER, -1)
    peaks = mine[:, :, D]
    peak = jnp.max(peaks, axis=0)
    scale = jnp.exp(peaks - peak)
    sums = jnp.sum(mine[:, :, :D] * scale[:, :, None], axis=0)
    total = jnp.sum(mine[:, :, D + 1] * scale, axis=0)
    owned = jnp.concatenate(
        [sums, jnp.zeros((SLOTS_PER, 128), jnp.float32).at[:, 0].set(peak).at[:, 1].set(total)], axis=1
    )
    owned = butterfly_softmax_sum(owned, "pos")
    slot_in = (owned[:, :D] / owned[:, D + 1 : D + 2]).astype(jnp.bfloat16)
    hidden = jax.nn.gelu(
        jnp.dot(slot_in, w_in[0], preferred_element_type=jnp.float32), approximate=True
    ).astype(jnp.bfloat16)
    expert_term = jnp.dot(hidden, w_out[0], preferred_element_type=jnp.float32)
    slot_out = butterfly_sum(expert_term, "pos").astype(jnp.bfloat16)
    row_peak = jnp.max(logits, axis=1, keepdims=True)
    row_weights = jnp.exp(logits - row_peak)
    combine = (row_weights / jnp.sum(row_weights, axis=1, keepdims=True)).astype(jnp.bfloat16)
    mixed = jnp.dot(
        combine,
        lax.all_gather(slot_out, "exp", axis=0, tiled=True),
        preferred_element_type=jnp.float32,
    )
    return jnp.swapaxes(mixed.astype(jnp.bfloat16).reshape(periods, channels, D), 0, 1)


def solution(mesh):
    in_specs = (
        P(("pos", "exp"), None, None),
        P(),
        P(),
        P("exp", None, "pos"),
        P("exp", "pos", None),
    )
    out_specs = P(("pos", "exp"), None, None)
    return jax.shard_map(
        per_device, mesh=mesh, in_specs=in_specs, out_specs=out_specs, check_vma=False
    )
```

```python
import jax
import jax.numpy as jnp
from jax import lax
from jax.sharding import PartitionSpec as P

D = 2048
SLOTS_PER = 8


def with_halo(array, sides, width):
    for axis, dim in sides:
        count, length = (lax.axis_size(axis), array.shape[dim])
        up = [(i, (i + 1) % count) for i in range(count - 1)]
        down = [(j, i) for i, j in up]
        last = lax.slice_in_dim(array, length - width, length, axis=dim)
        initial = lax.slice_in_dim(array, 0, width, axis=dim)
        before = lax.ppermute(last, axis, up)
        after = lax.ppermute(initial, axis, down)
        array = jnp.concatenate([before, array, after], axis=dim)
    return array


def butterfly_sum(value, axis):
    count = lax.axis_size(axis)
    step = 1
    while step < count:
        pairs = [(i, i ^ step) for i in range(count)]
        value = value + lax.ppermute(value, axis, pairs)
        step *= 2
    return value


def merge(mine, theirs):
    peak = jnp.maximum(mine[:, D], theirs[:, D])
    a = jnp.exp(mine[:, D] - peak)[:, None]
    b = jnp.exp(theirs[:, D] - peak)[:, None]
    merged = mine * a + theirs * b
    return merged.at[:, D].set(peak)


def butterfly_softmax_sum(value, axis):
    count = lax.axis_size(axis)
    step = 1
    while step < count:
        pairs = [(i, i ^ step) for i in range(count)]
        value = merge(value, lax.ppermute(value, axis, pairs))
        step *= 2
    return value


def exchange(value, axis):
    count = lax.axis_size(axis)
    spread = jnp.broadcast_to(value[None], (count,) + value.shape)
    return lax.all_to_all(spread, axis, 0, 0, tiled=True)


def merge_all(blocks):
    peaks = blocks[:, :, D]
    peak = jnp.max(peaks, axis=0)
    scale = jnp.exp(peaks - peak)
    sums = jnp.sum(blocks[:, :, :D] * scale[:, :, None], axis=0)
    total = jnp.sum(blocks[:, :, D + 1] * scale, axis=0)
    extra = jnp.zeros((blocks.shape[1], blocks.shape[2] - D), jnp.float32)
    return jnp.concatenate([sums, extra.at[:, 0].set(peak).at[:, 1].set(total)], axis=1)


def per_device(patches, conv_weight, phi, w_in, w_out):
    channels, periods, samples = patches.shape
    every = ("pos", "exp")
    padded = with_halo(jnp.swapaxes(patches, 0, 1), ((every, 1),), 1)
    window = jnp.concatenate([padded[:, offset : offset + channels] for offset in range(3)], axis=2)
    window = window.reshape(periods * channels, 3 * samples)
    taps = conv_weight.reshape(3 * samples, D)
    flat = jnp.dot(window, taps, preferred_element_type=jnp.float32).astype(jnp.bfloat16)
    logits = jnp.dot(flat, phi, preferred_element_type=jnp.float32)
    slots = logits.shape[1]

    local_peak = jnp.max(logits, axis=0)
    raw_weights = jnp.exp(logits - local_peak)
    local_total = jnp.sum(raw_weights, axis=0)
    every_slot = lax.dot_general(
        raw_weights.astype(jnp.bfloat16), flat, (((0,), (0,)), ((), ())),
        preferred_element_type=jnp.float32,
    )
    extra = jnp.zeros((slots, 128), jnp.float32)
    extra = extra.at[:, 0].set(local_peak).at[:, 1].set(local_total)
    packed = jnp.concatenate([every_slot, extra], axis=1)
    groups = lax.axis_size("exp")
    mine = lax.all_to_all(packed, "exp", 0, 0, tiled=True).reshape(groups, SLOTS_PER, -1)
    owned = merge_all(mine)
    owned = merge_all(exchange(owned, "pos"))
    slot_in = (owned[:, :D] / owned[:, D + 1 : D + 2]).astype(jnp.bfloat16)
    hidden = jax.nn.gelu(
        jnp.dot(slot_in, w_in[0], preferred_element_type=jnp.float32), approximate=True
    ).astype(jnp.bfloat16)
    expert_term = jnp.dot(hidden, w_out[0], preferred_element_type=jnp.float32)
    slot_out = jnp.sum(exchange(expert_term, "pos"), axis=0).astype(jnp.bfloat16)
    row_peak = jnp.max(logits, axis=1, keepdims=True)
    row_weights = jnp.exp(logits - row_peak)
    combine = (row_weights / jnp.sum(row_weights, axis=1, keepdims=True)).astype(jnp.bfloat16)
    mixed = jnp.dot(
        combine,
        lax.all_gather(slot_out, "exp", axis=0, tiled=True),
        preferred_element_type=jnp.float32,
    )
    return jnp.swapaxes(mixed.astype(jnp.bfloat16).reshape(periods, channels, D), 0, 1)


def solution(mesh):
    in_specs = (
        P(("pos", "exp"), None, None),
        P(),
        P(),
        P("exp", None, "pos"),
        P("exp", "pos", None),
    )
    out_specs = P(("pos", "exp"), None, None)
    return jax.shard_map(
        per_device, mesh=mesh, in_specs=in_specs, out_specs=out_specs, check_vma=False
    )
```

```python
import jax
import jax.numpy as jnp
from jax import lax
from jax.experimental import pallas as pl
from jax.sharding import PartitionSpec as P

D = 2048
SLOTS_PER = 8


def with_halo(array, sides, width):
    for axis, dim in sides:
        count, length = (lax.axis_size(axis), array.shape[dim])
        up = [(i, (i + 1) % count) for i in range(count - 1)]
        down = [(j, i) for i, j in up]
        last = lax.slice_in_dim(array, length - width, length, axis=dim)
        initial = lax.slice_in_dim(array, 0, width, axis=dim)
        before = lax.ppermute(last, axis, up)
        after = lax.ppermute(initial, axis, down)
        array = jnp.concatenate([before, array, after], axis=dim)
    return array


def butterfly_sum(value, axis):
    count = lax.axis_size(axis)
    step = 1
    while step < count:
        pairs = [(i, i ^ step) for i in range(count)]
        value = value + lax.ppermute(value, axis, pairs)
        step *= 2
    return value


def merge(mine, theirs):
    peak = jnp.maximum(mine[:, D], theirs[:, D])
    a = jnp.exp(mine[:, D] - peak)[:, None]
    b = jnp.exp(theirs[:, D] - peak)[:, None]
    merged = mine * a + theirs * b
    return merged.at[:, D].set(peak)


def butterfly_softmax_sum(value, axis):
    count = lax.axis_size(axis)
    step = 1
    while step < count:
        pairs = [(i, i ^ step) for i in range(count)]
        value = merge(value, lax.ppermute(value, axis, pairs))
        step *= 2
    return value


def mix_kernel(combine_ref, slots_ref, out_ref):
    for period in range(combine_ref.shape[0]):
        part = jnp.dot(combine_ref[period], slots_ref[...], preferred_element_type=jnp.float32)
        out_ref[:, period, :] = part.astype(out_ref.dtype)


def mix(combine, slot_all, block=64):
    periods, channels, slots = combine.shape
    width = slot_all.shape[1]
    return pl.pallas_call(
        mix_kernel,
        grid=(channels // block,),
        in_specs=[
            pl.BlockSpec((periods, block, slots), lambda i: (0, i, 0)),
            pl.BlockSpec((slots, width), lambda i: (0, 0)),
        ],
        out_specs=pl.BlockSpec((block, periods, width), lambda i: (i, 0, 0)),
        out_shape=jax.ShapeDtypeStruct((channels, periods, width), jnp.bfloat16),
        cost_estimate=pl.CostEstimate(
            flops=2 * periods * channels * slots * width,
            bytes_accessed=2 * (periods * channels * (slots + width) + slots * width),
            transcendentals=0,
        ),
    )(combine, slot_all)


def per_device(patches, conv_weight, phi, w_in, w_out):
    channels, periods, samples = patches.shape
    every = ("pos", "exp")
    padded = with_halo(jnp.swapaxes(patches, 0, 1), ((every, 1),), 1)
    window = jnp.concatenate([padded[:, offset : offset + channels] for offset in range(3)], axis=2)
    window = window.reshape(periods * channels, 3 * samples)
    taps = conv_weight.reshape(3 * samples, D)
    flat = jnp.dot(window, taps, preferred_element_type=jnp.float32).astype(jnp.bfloat16)
    logits = jnp.dot(flat, phi, preferred_element_type=jnp.float32)
    slots = logits.shape[1]

    local_peak = jnp.max(logits, axis=0)
    raw_weights = jnp.exp(logits - local_peak)
    local_total = jnp.sum(raw_weights, axis=0)
    every_slot = lax.dot_general(
        raw_weights.astype(jnp.bfloat16), flat, (((0,), (0,)), ((), ())),
        preferred_element_type=jnp.float32,
    )
    extra = jnp.zeros((slots, 128), jnp.float32)
    extra = extra.at[:, 0].set(local_peak).at[:, 1].set(local_total)
    packed = jnp.concatenate([every_slot, extra], axis=1)
    groups = lax.axis_size("exp")
    mine = lax.all_to_all(packed, "exp", 0, 0, tiled=True).reshape(groups, SLOTS_PER, -1)
    peaks = mine[:, :, D]
    peak = jnp.max(peaks, axis=0)
    scale = jnp.exp(peaks - peak)
    sums = jnp.sum(mine[:, :, :D] * scale[:, :, None], axis=0)
    total = jnp.sum(mine[:, :, D + 1] * scale, axis=0)
    owned = jnp.concatenate(
        [sums, jnp.zeros((SLOTS_PER, 128), jnp.float32).at[:, 0].set(peak).at[:, 1].set(total)], axis=1
    )
    owned = butterfly_softmax_sum(owned, "pos")
    slot_in = (owned[:, :D] / owned[:, D + 1 : D + 2]).astype(jnp.bfloat16)
    hidden = jax.nn.gelu(
        jnp.dot(slot_in, w_in[0], preferred_element_type=jnp.float32), approximate=True
    ).astype(jnp.bfloat16)
    expert_term = jnp.dot(hidden, w_out[0], preferred_element_type=jnp.float32)
    slot_out = butterfly_sum(expert_term, "pos").astype(jnp.bfloat16)
    row_peak = jnp.max(logits, axis=1, keepdims=True)
    row_weights = jnp.exp(logits - row_peak)
    combine = (row_weights / jnp.sum(row_weights, axis=1, keepdims=True)).astype(jnp.bfloat16)
    slot_all = lax.all_gather(slot_out, "exp", axis=0, tiled=True)
    return mix(combine.reshape(periods, channels, slots), slot_all)


def solution(mesh):
    in_specs = (
        P(("pos", "exp"), None, None),
        P(),
        P(),
        P("exp", None, "pos"),
        P("exp", "pos", None),
    )
    out_specs = P(("pos", "exp"), None, None)
    return jax.shard_map(
        per_device, mesh=mesh, in_specs=in_specs, out_specs=out_specs, check_vma=False
    )
```

```python
import jax
import jax.numpy as jnp
from jax import lax
from jax.experimental import pallas as pl
from jax.sharding import PartitionSpec as P

D = 2048
SLOTS_PER = 8


def with_halo(array, sides, width):
    for axis, dim in sides:
        count, length = (lax.axis_size(axis), array.shape[dim])
        up = [(i, (i + 1) % count) for i in range(count - 1)]
        down = [(j, i) for i, j in up]
        last = lax.slice_in_dim(array, length - width, length, axis=dim)
        initial = lax.slice_in_dim(array, 0, width, axis=dim)
        before = lax.ppermute(last, axis, up)
        after = lax.ppermute(initial, axis, down)
        array = jnp.concatenate([before, array, after], axis=dim)
    return array


def butterfly_sum(value, axis):
    count = lax.axis_size(axis)
    step = 1
    while step < count:
        pairs = [(i, i ^ step) for i in range(count)]
        value = value + lax.ppermute(value, axis, pairs)
        step *= 2
    return value


def merge(mine, theirs):
    peak = jnp.maximum(mine[:, D], theirs[:, D])
    a = jnp.exp(mine[:, D] - peak)[:, None]
    b = jnp.exp(theirs[:, D] - peak)[:, None]
    merged = mine * a + theirs * b
    return merged.at[:, D].set(peak)


def butterfly_softmax_sum(value, axis):
    count = lax.axis_size(axis)
    step = 1
    while step < count:
        pairs = [(i, i ^ step) for i in range(count)]
        value = merge(value, lax.ppermute(value, axis, pairs))
        step *= 2
    return value


def mix_kernel(combine_ref, slots_ref, out_ref):
    part = jnp.dot(combine_ref[...], slots_ref[...], preferred_element_type=jnp.float32)
    out_ref[...] = part.astype(out_ref.dtype).reshape(out_ref.shape)


def mix(combine, slot_all, periods, block=64):
    rows, slots = combine.shape
    channels = rows // periods
    width = slot_all.shape[1]
    return pl.pallas_call(
        mix_kernel,
        grid=(channels // block,),
        in_specs=[
            pl.BlockSpec((block * periods, slots), lambda i: (i, 0)),
            pl.BlockSpec((slots, width), lambda i: (0, 0)),
        ],
        out_specs=pl.BlockSpec((block, periods, width), lambda i: (i, 0, 0)),
        out_shape=jax.ShapeDtypeStruct((channels, periods, width), jnp.bfloat16),
        cost_estimate=pl.CostEstimate(
            flops=2 * rows * slots * width,
            bytes_accessed=2 * (rows * (slots + width) + slots * width),
            transcendentals=0,
        ),
    )(combine, slot_all)


def per_device(patches, conv_weight, phi, w_in, w_out):
    channels, periods, samples = patches.shape
    every = ("pos", "exp")
    padded = with_halo(jnp.swapaxes(patches, 0, 1), ((every, 1),), 1)
    window = jnp.concatenate([padded[:, offset : offset + channels] for offset in range(3)], axis=2)
    window = window.reshape(periods * channels, 3 * samples)
    taps = conv_weight.reshape(3 * samples, D)
    flat = jnp.dot(window, taps, preferred_element_type=jnp.float32).astype(jnp.bfloat16)
    logits = jnp.dot(flat, phi, preferred_element_type=jnp.float32)
    slots = logits.shape[1]

    local_peak = jnp.max(logits, axis=0)
    raw_weights = jnp.exp(logits - local_peak)
    local_total = jnp.sum(raw_weights, axis=0)
    every_slot = lax.dot_general(
        raw_weights.astype(jnp.bfloat16), flat, (((0,), (0,)), ((), ())),
        preferred_element_type=jnp.float32,
    )
    extra = jnp.zeros((slots, 128), jnp.float32)
    extra = extra.at[:, 0].set(local_peak).at[:, 1].set(local_total)
    packed = jnp.concatenate([every_slot, extra], axis=1)
    groups = lax.axis_size("exp")
    mine = lax.all_to_all(packed, "exp", 0, 0, tiled=True).reshape(groups, SLOTS_PER, -1)
    peaks = mine[:, :, D]
    peak = jnp.max(peaks, axis=0)
    scale = jnp.exp(peaks - peak)
    sums = jnp.sum(mine[:, :, :D] * scale[:, :, None], axis=0)
    total = jnp.sum(mine[:, :, D + 1] * scale, axis=0)
    owned = jnp.concatenate(
        [sums, jnp.zeros((SLOTS_PER, 128), jnp.float32).at[:, 0].set(peak).at[:, 1].set(total)], axis=1
    )
    owned = butterfly_softmax_sum(owned, "pos")
    slot_in = (owned[:, :D] / owned[:, D + 1 : D + 2]).astype(jnp.bfloat16)
    hidden = jax.nn.gelu(
        jnp.dot(slot_in, w_in[0], preferred_element_type=jnp.float32), approximate=True
    ).astype(jnp.bfloat16)
    expert_term = jnp.dot(hidden, w_out[0], preferred_element_type=jnp.float32)
    slot_out = butterfly_sum(expert_term, "pos").astype(jnp.bfloat16)
    row_peak = jnp.max(logits, axis=1, keepdims=True)
    row_weights = jnp.exp(logits - row_peak)
    combine = (row_weights / jnp.sum(row_weights, axis=1, keepdims=True)).astype(jnp.bfloat16)
    slot_all = lax.all_gather(slot_out, "exp", axis=0, tiled=True)
    by_channel = jnp.swapaxes(combine.reshape(periods, channels, slots), 0, 1).reshape(channels * periods, slots)
    return mix(by_channel, slot_all, periods)


def solution(mesh):
    in_specs = (
        P(("pos", "exp"), None, None),
        P(),
        P(),
        P("exp", None, "pos"),
        P("exp", "pos", None),
    )
    out_specs = P(("pos", "exp"), None, None)
    return jax.shard_map(
        per_device, mesh=mesh, in_specs=in_specs, out_specs=out_specs, check_vma=False
    )
```

```python
import jax
import jax.numpy as jnp
from jax import lax
from jax.experimental import pallas as pl
from jax.sharding import PartitionSpec as P

D = 2048
SLOTS_PER = 8


def with_halo(array, sides, width):
    for axis, dim in sides:
        count, length = (lax.axis_size(axis), array.shape[dim])
        up = [(i, (i + 1) % count) for i in range(count - 1)]
        down = [(j, i) for i, j in up]
        last = lax.slice_in_dim(array, length - width, length, axis=dim)
        initial = lax.slice_in_dim(array, 0, width, axis=dim)
        before = lax.ppermute(last, axis, up)
        after = lax.ppermute(initial, axis, down)
        array = jnp.concatenate([before, array, after], axis=dim)
    return array


def butterfly_sum(value, axis):
    count = lax.axis_size(axis)
    step = 1
    while step < count:
        pairs = [(i, i ^ step) for i in range(count)]
        value = value + lax.ppermute(value, axis, pairs)
        step *= 2
    return value


def merge(mine, theirs):
    peak = jnp.maximum(mine[:, D], theirs[:, D])
    a = jnp.exp(mine[:, D] - peak)[:, None]
    b = jnp.exp(theirs[:, D] - peak)[:, None]
    merged = mine * a + theirs * b
    return merged.at[:, D].set(peak)


def butterfly_softmax_sum(value, axis):
    count = lax.axis_size(axis)
    step = 1
    while step < count:
        pairs = [(i, i ^ step) for i in range(count)]
        value = merge(value, lax.ppermute(value, axis, pairs))
        step *= 2
    return value


def mix_kernel(combine_ref, slots_ref, out_ref):
    part = jnp.dot(combine_ref[...], slots_ref[...], preferred_element_type=jnp.float32)
    out_ref[...] = part.astype(out_ref.dtype).reshape(out_ref.shape)


def mix(combine, slot_all, periods, block=64):
    rows, slots = combine.shape
    channels = rows // periods
    width = slot_all.shape[1]
    return pl.pallas_call(
        mix_kernel,
        grid=(channels // block,),
        in_specs=[
            pl.BlockSpec((block * periods, slots), lambda i: (i, 0)),
            pl.BlockSpec((slots, width), lambda i: (0, 0)),
        ],
        out_specs=pl.BlockSpec((block, periods, width), lambda i: (i, 0, 0)),
        out_shape=jax.ShapeDtypeStruct((channels, periods, width), jnp.bfloat16),
        cost_estimate=pl.CostEstimate(
            flops=2 * rows * slots * width,
            bytes_accessed=2 * (rows * (slots + width) + slots * width),
            transcendentals=0,
        ),
    )(combine, slot_all)


def per_device(patches, conv_weight, phi, w_in, w_out):
    channels, periods, samples = patches.shape
    every = ("pos", "exp")
    by_period = jnp.swapaxes(patches, 0, 1)
    taps = conv_weight.reshape(3 * samples, D)
    padded = jnp.pad(by_period, ((0, 0), (1, 1), (0, 0)))
    window = jnp.concatenate([padded[:, offset : offset + channels] for offset in range(3)], axis=2)
    window = window.reshape(periods * channels, 3 * samples)
    flat = jnp.dot(window, taps, preferred_element_type=jnp.float32).astype(jnp.bfloat16)
    flat, first, last = lax.optimization_barrier((flat, by_period[:, :1], by_period[:, -1:]))
    count = lax.axis_size(every)
    up = [(i, i + 1) for i in range(count - 1)]
    before = lax.ppermute(last, every, up)
    after = lax.ppermute(first, every, [(j, i) for i, j in up])
    edges = jnp.concatenate(
        [
            jnp.concatenate([before, by_period[:, 0:2]], axis=1),
            jnp.concatenate([by_period[:, -2:], after], axis=1),
        ],
        axis=0,
    ).reshape(2 * periods, 3 * samples)
    edge_rows = jnp.dot(edges, taps, preferred_element_type=jnp.float32).astype(jnp.bfloat16)
    flat = flat.reshape(periods, channels, D)
    flat = flat.at[:, 0].set(edge_rows[:periods]).at[:, channels - 1].set(edge_rows[periods:])
    flat = flat.reshape(periods * channels, D)
    logits = jnp.dot(flat, phi, preferred_element_type=jnp.float32)
    slots = logits.shape[1]

    local_peak = jnp.max(logits, axis=0)
    raw_weights = jnp.exp(logits - local_peak)
    local_total = jnp.sum(raw_weights, axis=0)
    every_slot = lax.dot_general(
        raw_weights.astype(jnp.bfloat16), flat, (((0,), (0,)), ((), ())),
        preferred_element_type=jnp.float32,
    )
    extra = jnp.zeros((slots, 128), jnp.float32)
    extra = extra.at[:, 0].set(local_peak).at[:, 1].set(local_total)
    packed = jnp.concatenate([every_slot, extra], axis=1)
    groups = lax.axis_size("exp")
    mine = lax.all_to_all(packed, "exp", 0, 0, tiled=True).reshape(groups, SLOTS_PER, -1)
    peaks = mine[:, :, D]
    peak = jnp.max(peaks, axis=0)
    scale = jnp.exp(peaks - peak)
    sums = jnp.sum(mine[:, :, :D] * scale[:, :, None], axis=0)
    total = jnp.sum(mine[:, :, D + 1] * scale, axis=0)
    owned = jnp.concatenate(
        [sums, jnp.zeros((SLOTS_PER, 128), jnp.float32).at[:, 0].set(peak).at[:, 1].set(total)], axis=1
    )
    owned = butterfly_softmax_sum(owned, "pos")
    slot_in = (owned[:, :D] / owned[:, D + 1 : D + 2]).astype(jnp.bfloat16)
    hidden = jax.nn.gelu(
        jnp.dot(slot_in, w_in[0], preferred_element_type=jnp.float32), approximate=True
    ).astype(jnp.bfloat16)
    expert_term = jnp.dot(hidden, w_out[0], preferred_element_type=jnp.float32)
    slot_out = butterfly_sum(expert_term, "pos").astype(jnp.bfloat16)
    row_peak = jnp.max(logits, axis=1, keepdims=True)
    row_weights = jnp.exp(logits - row_peak)
    combine = (row_weights / jnp.sum(row_weights, axis=1, keepdims=True)).astype(jnp.bfloat16)
    slot_all = lax.all_gather(slot_out, "exp", axis=0, tiled=True)
    by_channel = jnp.swapaxes(combine.reshape(periods, channels, slots), 0, 1).reshape(channels * periods, slots)
    return mix(by_channel, slot_all, periods)


def solution(mesh):
    in_specs = (
        P(("pos", "exp"), None, None),
        P(),
        P(),
        P("exp", None, "pos"),
        P("exp", "pos", None),
    )
    out_specs = P(("pos", "exp"), None, None)
    return jax.shard_map(
        per_device, mesh=mesh, in_specs=in_specs, out_specs=out_specs, check_vma=False
    )
```

```python
import jax
import jax.numpy as jnp
from jax import lax
from jax.experimental import pallas as pl
from jax.sharding import PartitionSpec as P

D = 2048
SLOTS_PER = 8


def with_halo(array, sides, width):
    for axis, dim in sides:
        count, length = (lax.axis_size(axis), array.shape[dim])
        up = [(i, (i + 1) % count) for i in range(count - 1)]
        down = [(j, i) for i, j in up]
        last = lax.slice_in_dim(array, length - width, length, axis=dim)
        initial = lax.slice_in_dim(array, 0, width, axis=dim)
        before = lax.ppermute(last, axis, up)
        after = lax.ppermute(initial, axis, down)
        array = jnp.concatenate([before, array, after], axis=dim)
    return array


def butterfly_sum(value, axis):
    count = lax.axis_size(axis)
    step = 1
    while step < count:
        pairs = [(i, i ^ step) for i in range(count)]
        value = value + lax.ppermute(value, axis, pairs)
        step *= 2
    return value


def merge(mine, theirs):
    peak = jnp.maximum(mine[:, D : D + 1], theirs[:, D : D + 1])
    merged = mine * jnp.exp(mine[:, D : D + 1] - peak) + theirs * jnp.exp(theirs[:, D : D + 1] - peak)
    column = lax.broadcasted_iota(jnp.int32, mine.shape, 1)
    return jnp.where(column == D, peak, merged)


def butterfly_softmax_sum(value, axis):
    count = lax.axis_size(axis)
    step = 1
    while step < count:
        pairs = [(i, i ^ step) for i in range(count)]
        value = merge(value, lax.ppermute(value, axis, pairs))
        step *= 2
    return value


def mix_kernel(combine_ref, slots_ref, out_ref):
    part = jnp.dot(combine_ref[...], slots_ref[...], preferred_element_type=jnp.float32)
    out_ref[...] = part.astype(out_ref.dtype).reshape(out_ref.shape)


def mix(combine, slot_all, periods, block=128):
    rows, slots = combine.shape
    channels = rows // periods
    width = slot_all.shape[1]
    return pl.pallas_call(
        mix_kernel,
        grid=(channels // block,),
        in_specs=[
            pl.BlockSpec((block * periods, slots), lambda i: (i, 0)),
            pl.BlockSpec((slots, width), lambda i: (0, 0)),
        ],
        out_specs=pl.BlockSpec((block, periods, width), lambda i: (i, 0, 0)),
        out_shape=jax.ShapeDtypeStruct((channels, periods, width), jnp.bfloat16),
        cost_estimate=pl.CostEstimate(
            flops=2 * rows * slots * width,
            bytes_accessed=2 * (rows * (slots + width) + slots * width),
            transcendentals=0,
        ),
    )(combine, slot_all)


def per_device(patches, conv_weight, phi, w_in, w_out):
    channels, periods, samples = patches.shape
    every = ("pos", "exp")
    padded = with_halo(jnp.swapaxes(patches, 0, 1), ((every, 1),), 1)
    window = jnp.concatenate([padded[:, offset : offset + channels] for offset in range(3)], axis=2)
    window = window.reshape(periods * channels, 3 * samples)
    taps = conv_weight.reshape(3 * samples, D)
    flat = jnp.dot(window, taps, preferred_element_type=jnp.float32).astype(jnp.bfloat16)
    logits = jnp.dot(flat, phi, preferred_element_type=jnp.float32)
    slots = logits.shape[1]

    local_peak = jnp.max(logits, axis=0)
    raw_weights = jnp.exp(logits - local_peak)
    local_total = jnp.sum(raw_weights, axis=0)
    every_slot = lax.dot_general(
        raw_weights.astype(jnp.bfloat16), flat, (((0,), (0,)), ((), ())),
        preferred_element_type=jnp.float32,
    )
    extra = jnp.zeros((slots, 128), jnp.float32)
    extra = extra.at[:, 0].set(local_peak).at[:, 1].set(local_total)
    packed = jnp.concatenate([every_slot, extra], axis=1)
    groups = lax.axis_size("exp")
    mine = lax.all_to_all(packed, "exp", 0, 0, tiled=True).reshape(groups, SLOTS_PER, -1)
    peaks = mine[:, :, D]
    peak = jnp.max(peaks, axis=0)
    scale = jnp.exp(peaks - peak)
    sums = jnp.sum(mine[:, :, :D] * scale[:, :, None], axis=0)
    total = jnp.sum(mine[:, :, D + 1] * scale, axis=0)
    owned = jnp.concatenate(
        [sums, jnp.zeros((SLOTS_PER, 128), jnp.float32).at[:, 0].set(peak).at[:, 1].set(total)], axis=1
    )
    owned = butterfly_softmax_sum(owned, "pos")
    slot_in = (owned[:, :D] / owned[:, D + 1 : D + 2]).astype(jnp.bfloat16)
    hidden = jax.nn.gelu(
        jnp.dot(slot_in, w_in[0], preferred_element_type=jnp.float32), approximate=True
    ).astype(jnp.bfloat16)
    expert_term = jnp.dot(hidden, w_out[0], preferred_element_type=jnp.float32)
    slot_out = butterfly_sum(expert_term, "pos").astype(jnp.bfloat16)
    row_peak = jnp.max(logits, axis=1, keepdims=True)
    row_weights = jnp.exp(logits - row_peak)
    combine = (row_weights / jnp.sum(row_weights, axis=1, keepdims=True)).astype(jnp.bfloat16)
    slot_all = lax.all_gather(slot_out, "exp", axis=0, tiled=True)
    by_channel = jnp.swapaxes(combine.reshape(periods, channels, slots), 0, 1).reshape(channels * periods, slots)
    return mix(by_channel, slot_all, periods)


def solution(mesh):
    in_specs = (
        P(("pos", "exp"), None, None),
        P(),
        P(),
        P("exp", None, "pos"),
        P("exp", "pos", None),
    )
    out_specs = P(("pos", "exp"), None, None)
    return jax.shard_map(
        per_device, mesh=mesh, in_specs=in_specs, out_specs=out_specs, check_vma=False
    )
```

```python
import jax
import jax.numpy as jnp
from jax import lax
from jax.experimental import pallas as pl
from jax.sharding import PartitionSpec as P

D = 2048
SLOTS_PER = 8


def with_halo(array, sides, width):
    for axis, dim in sides:
        count, length = (lax.axis_size(axis), array.shape[dim])
        up = [(i, (i + 1) % count) for i in range(count - 1)]
        down = [(j, i) for i, j in up]
        last = lax.slice_in_dim(array, length - width, length, axis=dim)
        initial = lax.slice_in_dim(array, 0, width, axis=dim)
        before = lax.ppermute(last, axis, up)
        after = lax.ppermute(initial, axis, down)
        array = jnp.concatenate([before, array, after], axis=dim)
    return array


def butterfly_sum(value, axis):
    count = lax.axis_size(axis)
    step = 1
    while step < count:
        pairs = [(i, i ^ step) for i in range(count)]
        value = value + lax.ppermute(value, axis, pairs)
        step *= 2
    return value


def merge(mine, theirs):
    peak = jnp.maximum(mine[:, D : D + 1], theirs[:, D : D + 1])
    merged = mine * jnp.exp(mine[:, D : D + 1] - peak) + theirs * jnp.exp(theirs[:, D : D + 1] - peak)
    column = lax.broadcasted_iota(jnp.int32, mine.shape, 1)
    return jnp.where(column == D, peak, merged)


def butterfly_softmax_sum(value, axis):
    count = lax.axis_size(axis)
    step = 1
    while step < count:
        pairs = [(i, i ^ step) for i in range(count)]
        value = merge(value, lax.ppermute(value, axis, pairs))
        step *= 2
    return value


def mix_kernel(combine_ref, slots_ref, out_ref):
    part = jnp.dot(combine_ref[...], slots_ref[...], preferred_element_type=jnp.float32)
    out_ref[...] = part.astype(out_ref.dtype).reshape(out_ref.shape)


def mix(combine, slot_all, periods, block=256):
    rows, slots = combine.shape
    channels = rows // periods
    width = slot_all.shape[1]
    return pl.pallas_call(
        mix_kernel,
        grid=(channels // block,),
        in_specs=[
            pl.BlockSpec((block * periods, slots), lambda i: (i, 0)),
            pl.BlockSpec((slots, width), lambda i: (0, 0)),
        ],
        out_specs=pl.BlockSpec((block, periods, width), lambda i: (i, 0, 0)),
        out_shape=jax.ShapeDtypeStruct((channels, periods, width), jnp.bfloat16),
        cost_estimate=pl.CostEstimate(
            flops=2 * rows * slots * width,
            bytes_accessed=2 * (rows * (slots + width) + slots * width),
            transcendentals=0,
        ),
    )(combine, slot_all)


def per_device(patches, conv_weight, phi, w_in, w_out):
    channels, periods, samples = patches.shape
    every = ("pos", "exp")
    padded = with_halo(jnp.swapaxes(patches, 0, 1), ((every, 1),), 1)
    window = jnp.concatenate([padded[:, offset : offset + channels] for offset in range(3)], axis=2)
    window = window.reshape(periods * channels, 3 * samples)
    taps = conv_weight.reshape(3 * samples, D)
    flat = jnp.dot(window, taps, preferred_element_type=jnp.float32).astype(jnp.bfloat16)
    logits = jnp.dot(flat, phi, preferred_element_type=jnp.float32)
    slots = logits.shape[1]

    local_peak = jnp.max(logits, axis=0)
    raw_weights = jnp.exp(logits - local_peak)
    local_total = jnp.sum(raw_weights, axis=0)
    every_slot = lax.dot_general(
        raw_weights.astype(jnp.bfloat16), flat, (((0,), (0,)), ((), ())),
        preferred_element_type=jnp.float32,
    )
    extra = jnp.zeros((slots, 128), jnp.float32)
    extra = extra.at[:, 0].set(local_peak).at[:, 1].set(local_total)
    packed = jnp.concatenate([every_slot, extra], axis=1)
    groups = lax.axis_size("exp")
    mine = lax.all_to_all(packed, "exp", 0, 0, tiled=True).reshape(groups, SLOTS_PER, -1)
    peaks = mine[:, :, D]
    peak = jnp.max(peaks, axis=0)
    scale = jnp.exp(peaks - peak)
    sums = jnp.sum(mine[:, :, :D] * scale[:, :, None], axis=0)
    total = jnp.sum(mine[:, :, D + 1] * scale, axis=0)
    owned = jnp.concatenate(
        [sums, jnp.zeros((SLOTS_PER, 128), jnp.float32).at[:, 0].set(peak).at[:, 1].set(total)], axis=1
    )
    owned = butterfly_softmax_sum(owned, "pos")
    slot_in = (owned[:, :D] / owned[:, D + 1 : D + 2]).astype(jnp.bfloat16)
    hidden = jax.nn.gelu(
        jnp.dot(slot_in, w_in[0], preferred_element_type=jnp.float32), approximate=True
    ).astype(jnp.bfloat16)
    expert_term = jnp.dot(hidden, w_out[0], preferred_element_type=jnp.float32)
    slot_out = butterfly_sum(expert_term, "pos").astype(jnp.bfloat16)
    row_peak = jnp.max(logits, axis=1, keepdims=True)
    row_weights = jnp.exp(logits - row_peak)
    combine = (row_weights / jnp.sum(row_weights, axis=1, keepdims=True)).astype(jnp.bfloat16)
    slot_all = lax.all_gather(slot_out, "exp", axis=0, tiled=True)
    by_channel = jnp.swapaxes(combine.reshape(periods, channels, slots), 0, 1).reshape(channels * periods, slots)
    return mix(by_channel, slot_all, periods)


def solution(mesh):
    in_specs = (
        P(("pos", "exp"), None, None),
        P(),
        P(),
        P("exp", None, "pos"),
        P("exp", "pos", None),
    )
    out_specs = P(("pos", "exp"), None, None)
    return jax.shard_map(
        per_device, mesh=mesh, in_specs=in_specs, out_specs=out_specs, check_vma=False
    )
```

```python
import jax
import jax.numpy as jnp
from jax import lax
from jax.experimental import pallas as pl
from jax.sharding import PartitionSpec as P

D = 2048
SLOTS_PER = 8


def with_halo(array, sides, width):
    for axis, dim in sides:
        count, length = (lax.axis_size(axis), array.shape[dim])
        index = lax.axis_index(axis)
        up = [(i, (i + 1) % count) for i in range(count)]
        down = [(j, i) for i, j in up]
        last = lax.slice_in_dim(array, length - width, length, axis=dim)
        initial = lax.slice_in_dim(array, 0, width, axis=dim)
        before = jnp.where(index == 0, 0, lax.ppermute(last, axis, up)).astype(array.dtype)
        after = jnp.where(index == count - 1, 0, lax.ppermute(initial, axis, down)).astype(array.dtype)
        array = jnp.concatenate([before, array, after], axis=dim)
    return array


def butterfly_sum(value, axis):
    count = lax.axis_size(axis)
    step = 1
    while step < count:
        pairs = [(i, i ^ step) for i in range(count)]
        value = value + lax.ppermute(value, axis, pairs)
        step *= 2
    return value


def merge(mine, theirs):
    peak = jnp.maximum(mine[:, D : D + 1], theirs[:, D : D + 1])
    merged = mine * jnp.exp(mine[:, D : D + 1] - peak) + theirs * jnp.exp(theirs[:, D : D + 1] - peak)
    column = lax.broadcasted_iota(jnp.int32, mine.shape, 1)
    return jnp.where(column == D, peak, merged)


def butterfly_softmax_sum(value, axis):
    count = lax.axis_size(axis)
    step = 1
    while step < count:
        pairs = [(i, i ^ step) for i in range(count)]
        value = merge(value, lax.ppermute(value, axis, pairs))
        step *= 2
    return value


def mix_kernel(combine_ref, slots_ref, out_ref):
    part = jnp.dot(combine_ref[...], slots_ref[...], preferred_element_type=jnp.float32)
    out_ref[...] = part.astype(out_ref.dtype).reshape(out_ref.shape)


def mix(combine, slot_all, periods, block=128):
    rows, slots = combine.shape
    channels = rows // periods
    width = slot_all.shape[1]
    return pl.pallas_call(
        mix_kernel,
        grid=(channels // block,),
        in_specs=[
            pl.BlockSpec((block * periods, slots), lambda i: (i, 0)),
            pl.BlockSpec((slots, width), lambda i: (0, 0)),
        ],
        out_specs=pl.BlockSpec((block, periods, width), lambda i: (i, 0, 0)),
        out_shape=jax.ShapeDtypeStruct((channels, periods, width), jnp.bfloat16),
        cost_estimate=pl.CostEstimate(
            flops=2 * rows * slots * width,
            bytes_accessed=2 * (rows * (slots + width) + slots * width),
            transcendentals=0,
        ),
    )(combine, slot_all)


def per_device(patches, conv_weight, phi, w_in, w_out):
    channels, periods, samples = patches.shape
    every = ("pos", "exp")
    padded = with_halo(jnp.swapaxes(patches, 0, 1), ((every, 1),), 1)
    window = jnp.concatenate([padded[:, offset : offset + channels] for offset in range(3)], axis=2)
    window = window.reshape(periods * channels, 3 * samples)
    taps = conv_weight.reshape(3 * samples, D)
    flat = jnp.dot(window, taps, preferred_element_type=jnp.float32).astype(jnp.bfloat16)
    logits = jnp.dot(flat, phi, preferred_element_type=jnp.float32)
    slots = logits.shape[1]

    local_peak = jnp.max(logits, axis=0)
    raw_weights = jnp.exp(logits - local_peak)
    local_total = jnp.sum(raw_weights, axis=0)
    every_slot = lax.dot_general(
        raw_weights.astype(jnp.bfloat16), flat, (((0,), (0,)), ((), ())),
        preferred_element_type=jnp.float32,
    )
    extra = jnp.zeros((slots, 128), jnp.float32)
    extra = extra.at[:, 0].set(local_peak).at[:, 1].set(local_total)
    packed = jnp.concatenate([every_slot, extra], axis=1)
    groups = lax.axis_size("exp")
    mine = lax.all_to_all(packed, "exp", 0, 0, tiled=True).reshape(groups, SLOTS_PER, -1)
    peaks = mine[:, :, D]
    peak = jnp.max(peaks, axis=0)
    scale = jnp.exp(peaks - peak)
    sums = jnp.sum(mine[:, :, :D] * scale[:, :, None], axis=0)
    total = jnp.sum(mine[:, :, D + 1] * scale, axis=0)
    owned = jnp.concatenate(
        [sums, jnp.zeros((SLOTS_PER, 128), jnp.float32).at[:, 0].set(peak).at[:, 1].set(total)], axis=1
    )
    owned = butterfly_softmax_sum(owned, "pos")
    slot_in = (owned[:, :D] / owned[:, D + 1 : D + 2]).astype(jnp.bfloat16)
    hidden = jax.nn.gelu(
        jnp.dot(slot_in, w_in[0], preferred_element_type=jnp.float32), approximate=True
    ).astype(jnp.bfloat16)
    expert_term = jnp.dot(hidden, w_out[0], preferred_element_type=jnp.float32)
    slot_out = butterfly_sum(expert_term, "pos").astype(jnp.bfloat16)
    row_peak = jnp.max(logits, axis=1, keepdims=True)
    row_weights = jnp.exp(logits - row_peak)
    combine = (row_weights / jnp.sum(row_weights, axis=1, keepdims=True)).astype(jnp.bfloat16)
    slot_all = lax.all_gather(slot_out, "exp", axis=0, tiled=True)
    by_channel = jnp.swapaxes(combine.reshape(periods, channels, slots), 0, 1).reshape(channels * periods, slots)
    return mix(by_channel, slot_all, periods)


def solution(mesh):
    in_specs = (
        P(("pos", "exp"), None, None),
        P(),
        P(),
        P("exp", None, "pos"),
        P("exp", "pos", None),
    )
    out_specs = P(("pos", "exp"), None, None)
    return jax.shard_map(
        per_device, mesh=mesh, in_specs=in_specs, out_specs=out_specs, check_vma=False
    )
```

```python
import jax
import jax.numpy as jnp
from jax import lax
from jax.experimental import pallas as pl
from jax.sharding import PartitionSpec as P

D = 2048
SLOTS_PER = 8


def with_halo(array, sides, width):
    for axis, dim in sides:
        count, length = (lax.axis_size(axis), array.shape[dim])
        index = lax.axis_index(axis)
        up = [(i, (i + 1) % count) for i in range(count)]
        down = [(j, i) for i, j in up]
        last = lax.slice_in_dim(array, length - width, length, axis=dim)
        initial = lax.slice_in_dim(array, 0, width, axis=dim)
        before = jnp.where(index == 0, 0, lax.ppermute(last, axis, up)).astype(array.dtype)
        after = jnp.where(index == count - 1, 0, lax.ppermute(initial, axis, down)).astype(array.dtype)
        array = jnp.concatenate([before, array, after], axis=dim)
    return array


def butterfly_sum(value, axis):
    count = lax.axis_size(axis)
    step = count // 2
    while step >= 1:
        pairs = [(i, i ^ step) for i in range(count)]
        value = value + lax.ppermute(value, axis, pairs)
        step //= 2
    return value


def merge(mine, theirs):
    peak = jnp.maximum(mine[:, D : D + 1], theirs[:, D : D + 1])
    merged = mine * jnp.exp(mine[:, D : D + 1] - peak) + theirs * jnp.exp(theirs[:, D : D + 1] - peak)
    column = lax.broadcasted_iota(jnp.int32, mine.shape, 1)
    return jnp.where(column == D, peak, merged)


def butterfly_softmax_sum(value, axis):
    count = lax.axis_size(axis)
    step = count // 2
    while step >= 1:
        pairs = [(i, i ^ step) for i in range(count)]
        value = merge(value, lax.ppermute(value, axis, pairs))
        step //= 2
    return value


def mix_kernel(combine_ref, slots_ref, out_ref):
    part = jnp.dot(combine_ref[...], slots_ref[...], preferred_element_type=jnp.float32)
    out_ref[...] = part.astype(out_ref.dtype).reshape(out_ref.shape)


def mix(combine, slot_all, periods, block=128):
    rows, slots = combine.shape
    channels = rows // periods
    width = slot_all.shape[1]
    return pl.pallas_call(
        mix_kernel,
        grid=(channels // block,),
        in_specs=[
            pl.BlockSpec((block * periods, slots), lambda i: (i, 0)),
            pl.BlockSpec((slots, width), lambda i: (0, 0)),
        ],
        out_specs=pl.BlockSpec((block, periods, width), lambda i: (i, 0, 0)),
        out_shape=jax.ShapeDtypeStruct((channels, periods, width), jnp.bfloat16),
        cost_estimate=pl.CostEstimate(
            flops=2 * rows * slots * width,
            bytes_accessed=2 * (rows * (slots + width) + slots * width),
            transcendentals=0,
        ),
    )(combine, slot_all)


def per_device(patches, conv_weight, phi, w_in, w_out):
    channels, periods, samples = patches.shape
    every = ("pos", "exp")
    padded = with_halo(jnp.swapaxes(patches, 0, 1), ((every, 1),), 1)
    window = jnp.concatenate([padded[:, offset : offset + channels] for offset in range(3)], axis=2)
    window = window.reshape(periods * channels, 3 * samples)
    taps = conv_weight.reshape(3 * samples, D)
    flat = jnp.dot(window, taps, preferred_element_type=jnp.float32).astype(jnp.bfloat16)
    logits = jnp.dot(flat, phi, preferred_element_type=jnp.float32)
    slots = logits.shape[1]

    local_peak = jnp.max(logits, axis=0)
    raw_weights = jnp.exp(logits - local_peak)
    local_total = jnp.sum(raw_weights, axis=0)
    every_slot = lax.dot_general(
        raw_weights.astype(jnp.bfloat16), flat, (((0,), (0,)), ((), ())),
        preferred_element_type=jnp.float32,
    )
    extra = jnp.zeros((slots, 128), jnp.float32)
    extra = extra.at[:, 0].set(local_peak).at[:, 1].set(local_total)
    packed = jnp.concatenate([every_slot, extra], axis=1)
    groups = lax.axis_size("exp")
    mine = lax.all_to_all(packed, "exp", 0, 0, tiled=True).reshape(groups, SLOTS_PER, -1)
    peaks = mine[:, :, D]
    peak = jnp.max(peaks, axis=0)
    scale = jnp.exp(peaks - peak)
    sums = jnp.sum(mine[:, :, :D] * scale[:, :, None], axis=0)
    total = jnp.sum(mine[:, :, D + 1] * scale, axis=0)
    owned = jnp.concatenate(
        [sums, jnp.zeros((SLOTS_PER, 128), jnp.float32).at[:, 0].set(peak).at[:, 1].set(total)], axis=1
    )
    owned = butterfly_softmax_sum(owned, "pos")
    slot_in = (owned[:, :D] / owned[:, D + 1 : D + 2]).astype(jnp.bfloat16)
    hidden = jax.nn.gelu(
        jnp.dot(slot_in, w_in[0], preferred_element_type=jnp.float32), approximate=True
    ).astype(jnp.bfloat16)
    expert_term = jnp.dot(hidden, w_out[0], preferred_element_type=jnp.float32)
    slot_out = butterfly_sum(expert_term, "pos").astype(jnp.bfloat16)
    row_peak = jnp.max(logits, axis=1, keepdims=True)
    row_weights = jnp.exp(logits - row_peak)
    combine = (row_weights / jnp.sum(row_weights, axis=1, keepdims=True)).astype(jnp.bfloat16)
    slot_all = lax.all_gather(slot_out, "exp", axis=0, tiled=True)
    by_channel = jnp.swapaxes(combine.reshape(periods, channels, slots), 0, 1).reshape(channels * periods, slots)
    return mix(by_channel, slot_all, periods)


def solution(mesh):
    in_specs = (
        P(("pos", "exp"), None, None),
        P(),
        P(),
        P("exp", None, "pos"),
        P("exp", "pos", None),
    )
    out_specs = P(("pos", "exp"), None, None)
    return jax.shard_map(
        per_device, mesh=mesh, in_specs=in_specs, out_specs=out_specs, check_vma=False
    )
```

```python
import jax
import jax.numpy as jnp
from jax import lax
from jax.experimental import pallas as pl
from jax.sharding import PartitionSpec as P

D = 2048
SLOTS_PER = 8


def with_halo(array, sides, width):
    for axis, dim in sides:
        count, length = (lax.axis_size(axis), array.shape[dim])
        index = lax.axis_index(axis)
        up = [(i, (i + 1) % count) for i in range(count)]
        down = [(j, i) for i, j in up]
        last = lax.slice_in_dim(array, length - width, length, axis=dim)
        initial = lax.slice_in_dim(array, 0, width, axis=dim)
        before = jnp.where(index == 0, 0, lax.ppermute(last, axis, up)).astype(array.dtype)
        after = jnp.where(index == count - 1, 0, lax.ppermute(initial, axis, down)).astype(array.dtype)
        array = jnp.concatenate([before, array, after], axis=dim)
    return array


def butterfly_sum(value, axis):
    count = lax.axis_size(axis)
    step = 1
    while step < count:
        pairs = [(i, i ^ step) for i in range(count)]
        value = value + lax.ppermute(value, axis, pairs)
        step *= 2
    return value


def merge(mine, theirs):
    peak = jnp.maximum(mine[:, D : D + 1], theirs[:, D : D + 1])
    merged = mine * jnp.exp(mine[:, D : D + 1] - peak) + theirs * jnp.exp(theirs[:, D : D + 1] - peak)
    column = lax.broadcasted_iota(jnp.int32, mine.shape, 1)
    return jnp.where(column == D, peak, merged)


def butterfly_softmax_sum(value, axis):
    count = lax.axis_size(axis)
    step = 1
    while step < count:
        pairs = [(i, i ^ step) for i in range(count)]
        value = merge(value, lax.ppermute(value, axis, pairs))
        step *= 2
    return value


def mix_kernel(combine_ref, slots_ref, out_ref):
    part = jnp.dot(combine_ref[...], slots_ref[...], preferred_element_type=jnp.float32)
    out_ref[...] = part.astype(out_ref.dtype).reshape(out_ref.shape)


def mix(combine, slot_all, periods, block=128):
    rows, slots = combine.shape
    channels = rows // periods
    width = slot_all.shape[1]
    return pl.pallas_call(
        mix_kernel,
        grid=(channels // block,),
        in_specs=[
            pl.BlockSpec((block * periods, slots), lambda i: (i, 0)),
            pl.BlockSpec((slots, width), lambda i: (0, 0)),
        ],
        out_specs=pl.BlockSpec((block, periods, width), lambda i: (i, 0, 0)),
        out_shape=jax.ShapeDtypeStruct((channels, periods, width), jnp.bfloat16),
        cost_estimate=pl.CostEstimate(
            flops=2 * rows * slots * width,
            bytes_accessed=2 * (rows * (slots + width) + slots * width),
            transcendentals=0,
        ),
    )(combine, slot_all)


def pack(sums, peak, total):
    rows = sums.shape[0]
    column = lax.broadcasted_iota(jnp.int32, (rows, 128), 1)
    extra = jnp.where(column == 0, peak[:, None], jnp.where(column == 1, total[:, None], 0.0))
    return jnp.concatenate([sums, extra], axis=1)


def per_device(patches, conv_weight, phi, w_in, w_out):
    channels, periods, samples = patches.shape
    every = ("pos", "exp")
    padded = with_halo(jnp.swapaxes(patches, 0, 1), ((every, 1),), 1)
    window = jnp.concatenate([padded[:, offset : offset + channels] for offset in range(3)], axis=2)
    window = window.reshape(periods * channels, 3 * samples)
    taps = conv_weight.reshape(3 * samples, D)
    flat = jnp.dot(window, taps, preferred_element_type=jnp.float32).astype(jnp.bfloat16)
    logits = jnp.dot(flat, phi, preferred_element_type=jnp.float32)
    slots = logits.shape[1]

    local_peak = jnp.max(logits, axis=0)
    raw_weights = jnp.exp(logits - local_peak)
    local_total = jnp.sum(raw_weights, axis=0)
    every_slot = lax.dot_general(
        raw_weights.astype(jnp.bfloat16), flat, (((0,), (0,)), ((), ())),
        preferred_element_type=jnp.float32,
    )
    packed = pack(every_slot, local_peak, local_total)
    groups = lax.axis_size("exp")
    mine = lax.all_to_all(packed, "exp", 0, 0, tiled=True).reshape(groups, SLOTS_PER, -1)
    peaks = mine[:, :, D]
    peak = jnp.max(peaks, axis=0)
    scale = jnp.exp(peaks - peak)
    sums = jnp.sum(mine[:, :, :D] * scale[:, :, None], axis=0)
    total = jnp.sum(mine[:, :, D + 1] * scale, axis=0)
    owned = pack(sums, peak, total)
    owned = butterfly_softmax_sum(owned, "pos")
    slot_in = (owned[:, :D] / owned[:, D + 1 : D + 2]).astype(jnp.bfloat16)
    hidden = jax.nn.gelu(
        jnp.dot(slot_in, w_in[0], preferred_element_type=jnp.float32), approximate=True
    ).astype(jnp.bfloat16)
    expert_term = jnp.dot(hidden, w_out[0], preferred_element_type=jnp.float32)
    slot_out = butterfly_sum(expert_term, "pos").astype(jnp.bfloat16)
    row_peak = jnp.max(logits, axis=1, keepdims=True)
    row_weights = jnp.exp(logits - row_peak)
    combine = (row_weights / jnp.sum(row_weights, axis=1, keepdims=True)).astype(jnp.bfloat16)
    slot_all = lax.all_gather(slot_out, "exp", axis=0, tiled=True)
    by_channel = jnp.swapaxes(combine.reshape(periods, channels, slots), 0, 1).reshape(channels * periods, slots)
    return mix(by_channel, slot_all, periods)


def solution(mesh):
    in_specs = (
        P(("pos", "exp"), None, None),
        P(),
        P(),
        P("exp", None, "pos"),
        P("exp", "pos", None),
    )
    out_specs = P(("pos", "exp"), None, None)
    return jax.shard_map(
        per_device, mesh=mesh, in_specs=in_specs, out_specs=out_specs, check_vma=False
    )
```
